32 devices in a mesh: rep: 2 (over y), seq: 4 (over z), head: 4 (over x, core).
Axes of the slice: x: 2, y: 2, z: 4, core: 2. Of those that a mesh axis runs over, the one named last changes fastest.
Arguments:
- queries: bfloat16 [3072, 2560], P(('rep', 'seq'), 'head'), parts along dimension 0, may hold values from -16 to 16
- keys: bfloat16 [3072, 2560], P(('rep', 'seq'), 'head'), parts along dimension 0, may hold values from -6 to 6
- values: bfloat16 [3072, 2560], P(('rep', 'seq'), 'head'), parts along dimension 0, may hold values from -6 to 6
- out_weight: bfloat16 [2560, 5120], P('seq', 'head'), may hold values from -0.3125 to 0.3125
- neighbours: int32 [8, 27], P('rep'), parts along dimension 0, may hold values from -1 to 3, as said below
- clip_ids: int32 [3072], P(('rep', 'seq')), parts along dimension 0, may hold values from 0 to 1
Outputs:
- output: bfloat16 [3072, 5120], P(('rep', 'seq'), 'head'), parts along dimension 0
The draws below stay inside these ranges and needn't reach their ends.
There are 2 independent parts, one for each index of `rep`. The reference program is written for one: setup_inputs(seed, part) draws one part's arguments, and reference() takes and returns one part's arrays. A program takes and returns all parts, laid end to end along the dimension named above; an argument that names none is the same for every part. Nothing has to cross between parts.
Inputs may be any that keep to these rules, and one draw needn't show every extreme that they name: `neighbours`: column 9 (a + 1) + 3 (b + 1) + (c + 1) of row s, for a, b, c each -1, 0 or 1, is either -1 or s + a * 4 * 7 + b * 7 + c; column 13 of row s is s.
All inputs are finite; a program needn't handle non-finite values.
Results may differ from the reference program's by a relative error of at most 0.0058.
Values may be sent and summed in bfloat16 or wider, within the bound.
No kernel may reach another device: no remote copies, remote signals or barrier semaphores. Data moves between devices by JAX's collectives and lax.ppermute only.
A program may use at most 192 MiB of HBM per device.

```python
import math
import jax
import jax.numpy as jnp
from jax import lax

D = 5120
HEADS = 20
HD = 128
TILE_T = 6
TILE_H = 8
TILE_W = 8
TGH = 4
TGW = 7
TILE_TOK = 384
TOKENS = 1536


def draw_queries(key, part):
    spread = jnp.clip(2.5 * jax.random.normal(jax.random.fold_in(key, 11), (TOKENS, HEADS * HD)), -15.0, 15.0)
    return spread.astype(jnp.bfloat16)


def draw_keys(key, part):
    spread = jnp.clip(jax.random.normal(jax.random.fold_in(key, 13), (TOKENS, HEADS * HD)), -6.0, 6.0)
    return spread.astype(jnp.bfloat16)


def tile_layers():
    return (TOKENS // TILE_TOK + TGH * TGW - 1) // (TGH * TGW)


def clip_boundary(key):
    frame_total = tile_layers() * TILE_T
    return jax.random.randint(jax.random.fold_in(key, 29), (), 1, frame_total)


def draw_clip_ids(key, part):
    boundary = clip_boundary(key)
    positions = jnp.arange(TOKENS)
    layer = positions // TILE_TOK // (TGH * TGW)
    frame = layer * TILE_T + positions % TILE_TOK // (TILE_H * TILE_W)
    return (frame >= boundary).astype(jnp.int32)


def draw_neighbours(key, part):
    tile_count = TOKENS // TILE_TOK
    kept = jax.random.randint(jax.random.fold_in(key, 31), (tile_count, 27), 0, 4) != 0
    slots = jnp.arange(tile_count)
    layer = slots // (TGH * TGW)
    row_pos = slots // TGW % TGH
    col_pos = slots % TGW
    columns = []
    column_index = 0
    for layer_step in (-1, 0, 1):
        for row_step in (-1, 0, 1):
            for col_step in (-1, 0, 1):
                near_layer = layer + layer_step
                near_row = row_pos + row_step
                near_col = col_pos + col_step
                near_slot = near_layer * TGH * TGW + near_row * TGW + near_col
                inside = (near_layer >= 0) & (near_row >= 0) & (near_row < TGH) & (near_col >= 0) & (near_col < TGW) & (near_slot >= 0) & (near_slot < tile_count)
                if column_index != 13:
                    inside = inside & kept[:, column_index]
                columns.append(jnp.where(inside, near_slot, -1))
                column_index += 1
    return jnp.stack(columns, axis=1).astype(jnp.int32)


def shard_levels(key, dims, shards, smallest, top_value):
    def one(axis_at, parts):
        heights = jax.random.uniform(jax.random.fold_in(jax.random.fold_in(key, 6), axis_at), (parts,), jnp.float32, smallest / len(shards), top_value / len(shards))
        return jnp.repeat(jnp.exp(heights), dims[axis_at] // parts).reshape((-1,) + (1,) * (len(dims) - axis_at - 1))

    loudness = one(*shards[0])
    for cut in shards[1:]:
        loudness = loudness * one(*cut)
    return loudness


def bell_draw(own_key, shape, scale, reach, split=(), kind=jnp.bfloat16):
    values = scale * jax.random.normal(own_key, shape, jnp.float32)
    if split:
        values = values * shard_levels(own_key, shape, split, -0.22, 0.18)
    return jnp.clip(values, -reach, reach).astype(kind)


def setup_inputs(seed: int = 0, part: int = 0) -> dict:
    key_of = jax.random.split(jax.random.key(seed), 7)
    part_keys = jax.random.split(jax.random.fold_in(key_of[6], part), 7)
    return {
        "queries": draw_queries(jax.random.fold_in(jax.random.fold_in(key_of[6], part), 71), part),
        "keys": draw_keys(jax.random.fold_in(jax.random.fold_in(key_of[6], part), 71), part),
        "values": bell_draw(part_keys[2], (TOKENS, HEADS * HD), 1.0, 6.0, ((0, 4), (1, 4))),
        "out_weight": bell_draw(key_of[3], (HEADS * HD, D), (HEADS * HD // 8) ** -0.5, 0.3125, ((0, 4), (1, 4))),
        "neighbours": draw_neighbours(jax.random.fold_in(jax.random.fold_in(key_of[6], part), 71), part),
        "clip_ids": draw_clip_ids(jax.random.fold_in(jax.random.fold_in(key_of[6], part), 71), part),
    }


def attend_head(query_head, key_head, value_head, allowed):
    scores = jnp.dot(query_head, key_head.T, preferred_element_type=jnp.float32) * (1.0 / math.sqrt(HD))
    masked = jnp.where(allowed, scores, -1e+30)
    highest = lax.optimization_barrier(jnp.max(masked, axis=1, keepdims=True))
    raised = jnp.where(allowed, jnp.exp(masked - highest), 0.0)
    summed = lax.optimization_barrier(jnp.sum(raised, axis=1, keepdims=True))
    weights = (raised / summed).astype(jnp.bfloat16)
    return jnp.dot(weights, value_head, preferred_element_type=jnp.float32).astype(jnp.bfloat16)

def reference(queries, keys, values, out_weight, neighbours, clip_ids):
    tile_count = TOKENS // TILE_TOK
    query_tiles = queries.reshape(tile_count, TILE_TOK, HEADS, HD)
    key_tiles = keys.reshape(tile_count, TILE_TOK, HEADS, HD)
    value_tiles = values.reshape(tile_count, TILE_TOK, HEADS, HD)
    clip_tiles = clip_ids.reshape(tile_count, TILE_TOK)

    def one_tile(tile_index):
        window = neighbours[tile_index]
        clamped = jnp.maximum(window, 0).astype(jnp.int32)
        near_keys = key_tiles[clamped].reshape(27 * TILE_TOK, HEADS, HD)
        near_values = value_tiles[clamped].reshape(27 * TILE_TOK, HEADS, HD)
        near_clips = clip_tiles[clamped].reshape(27 * TILE_TOK)
        usable = jnp.repeat(window >= 0, TILE_TOK)
        own_clips = clip_tiles[tile_index]
        allowed = usable[None, :] & (own_clips[:, None] == near_clips[None, :])
        head_inputs = (jnp.swapaxes(query_tiles[tile_index], 0, 1), jnp.swapaxes(near_keys, 0, 1), jnp.swapaxes(near_values, 0, 1))
        per_head = lax.map(lambda triple: attend_head(triple[0], triple[1], triple[2], allowed), head_inputs)
        return jnp.swapaxes(per_head, 0, 1)
    attended = lax.map(one_tile, jnp.arange(tile_count, dtype=jnp.int32))
    attended = attended.reshape(TOKENS, HEADS * HD)
    return jnp.dot(attended, out_weight, preferred_element_type=jnp.float32).astype(jnp.bfloat16)
```

```python
import math

import jax
import jax.numpy as jnp
from jax import lax
from jax.sharding import PartitionSpec as P

HD = 128
TGH = 4
TGW = 7


def from_behind(value, axis, by):
    peers = lax.axis_size(axis)
    pairs = [(i, i + by) for i in range(peers) if 0 <= i + by < peers]
    return lax.ppermute(value, axis, pairs)


def attend_head(query_head, key_head, value_head, allowed):
    scores = lax.dot_general(
        query_head, key_head, (((1,), (1,)), ((), ())), preferred_element_type=jnp.float32
    ) * (1.0 / math.sqrt(query_head.shape[1]))
    masked = jnp.where(allowed, scores, -1e30)
    highest = jnp.max(masked, axis=1, keepdims=True)
    raised = jnp.where(allowed, jnp.exp(masked - highest), 0.0)
    summed = jnp.sum(raised, axis=1, keepdims=True)
    weights = (raised / summed).astype(jnp.bfloat16)
    return jnp.dot(weights, value_head, preferred_element_type=jnp.float32).astype(jnp.bfloat16)


def on_device(queries, keys, values, out_weight, neighbours, clip_ids):
    tile_rows = queries.shape[0]
    feature_width = queries.shape[1]
    seq_count = lax.axis_size("seq")
    layer_tiles = TGH * TGW
    every_offset = set()
    for layer_step in (-1, 0, 1):
        for row_step in (-1, 0, 1):
            for col_step in (-1, 0, 1):
                every_offset.add(layer_step * layer_tiles + row_step * TGW + col_step)
    distances = [offset for offset in sorted(every_offset) if 0 < offset < seq_count]
    weight_piece = lax.all_gather(out_weight, "seq", axis=0, tiled=True)
    key_list = [keys]
    value_list = [values]
    clip_list = [clip_ids]
    offsets = [0]
    for distance in distances:
        below_keys, below_values, below_clips = from_behind(
            (keys, values, clip_ids), "seq", distance
        )
        above_keys, above_values, above_clips = from_behind(
            (keys, values, clip_ids), "seq", -distance
        )
        key_list += [below_keys, above_keys]
        value_list += [below_values, above_values]
        clip_list += [below_clips, above_clips]
        offsets += [distance, -distance]
    key_stack = jnp.stack(key_list)
    value_stack = jnp.stack(value_list)
    clip_stack = jnp.stack(clip_list)
    blocks = key_stack.shape[0]
    position = lax.axis_index("seq")
    window_row = lax.dynamic_index_in_dim(neighbours, position, 0, keepdims=False)
    sources = position - jnp.asarray(offsets, dtype=jnp.int32)
    present = jnp.any(
        (window_row[None, :] == sources[:, None]) & (window_row[None, :] >= 0), axis=1
    )
    key_clips = clip_stack.reshape(blocks * tile_rows)
    allowed = jnp.repeat(present, tile_rows)[None, :] & (clip_ids[:, None] == key_clips[None, :])
    key_rows = key_stack.reshape(blocks * tile_rows, feature_width)
    value_rows = value_stack.reshape(blocks * tile_rows, feature_width)
    head_outputs = []
    for head_index in range(feature_width // HD):
        first_col = head_index * HD
        head_outputs.append(
            attend_head(
                queries[:, first_col : first_col + HD],
                key_rows[:, first_col : first_col + HD],
                value_rows[:, first_col : first_col + HD],
                allowed,
            )
        )
    attended = jnp.concatenate(head_outputs, axis=1)
    head_count = lax.axis_size("head")
    head_position = lax.axis_index("head")
    projected = jnp.zeros((tile_rows, weight_piece.shape[1]), jnp.float32)
    for shift in range(head_count):
        if shift == 0:
            piece = attended
        else:
            pairs = [(j, (j + shift) % head_count) for j in range(head_count)]
            piece = lax.ppermute(attended, "head", pairs)
        block = (head_position - shift) % head_count
        rows = lax.dynamic_slice_in_dim(weight_piece, block * feature_width, feature_width, axis=0)
        projected = projected + jnp.dot(piece, rows, preferred_element_type=jnp.float32)
    return projected.astype(jnp.bfloat16)


def solution(mesh):
    in_specs = (
        P(("rep", "seq"), "head"),
        P(("rep", "seq"), "head"),
        P(("rep", "seq"), "head"),
        P("seq", "head"),
        P("rep", None),
        P(("rep", "seq")),
    )
    out_specs = P(("rep", "seq"), "head")
    return jax.shard_map(
        on_device, mesh=mesh, in_specs=in_specs, out_specs=out_specs, check_vma=False
    )
```

```python
import math

import jax
import jax.numpy as jnp
from jax import lax
from jax.sharding import PartitionSpec as P

HD = 128
TGH = 4
TGW = 7


def from_behind(value, axis, by):
    peers = lax.axis_size(axis)
    pairs = [(i, i + by) for i in range(peers) if 0 <= i + by < peers]
    return lax.ppermute(value, axis, pairs)


def chunk_bounds(width, lanes=128, widths=(3, 2)):
    units = width // lanes
    bounds = []
    first = 0
    for part in widths:
        last = min(units, first // lanes + part) * lanes
        if last > first:
            bounds.append((first, last))
            first = last
    if first < width:
        bounds.append((first, width))
    return bounds


def attend_head(query_head, key_head, value_head, allowed):
    scores = lax.dot_general(
        query_head, key_head, (((1,), (1,)), ((), ())), preferred_element_type=jnp.float32
    ) * (1.0 / math.sqrt(query_head.shape[1]))
    masked = jnp.where(allowed, scores, -1e30)
    highest = jnp.max(masked, axis=1, keepdims=True)
    raised = jnp.where(allowed, jnp.exp(masked - highest), 0.0)
    summed = jnp.sum(raised, axis=1, keepdims=True)
    weights = (raised / summed).astype(jnp.bfloat16)
    return jnp.dot(weights, value_head, preferred_element_type=jnp.float32).astype(jnp.bfloat16)


def on_device(queries, keys, values, out_weight, neighbours, clip_ids):
    tile_rows = queries.shape[0]
    feature_width = queries.shape[1]
    seq_count = lax.axis_size("seq")
    layer_tiles = TGH * TGW
    every_offset = set()
    for layer_step in (-1, 0, 1):
        for row_step in (-1, 0, 1):
            for col_step in (-1, 0, 1):
                every_offset.add(layer_step * layer_tiles + row_step * TGW + col_step)
    distances = [offset for offset in sorted(every_offset) if 0 < offset < seq_count]
    rep_count = lax.axis_size("rep")
    rep_position = lax.axis_index("rep")
    half_width = out_weight.shape[1] // rep_count
    own_half = lax.dynamic_slice_in_dim(out_weight, rep_position * half_width, half_width, axis=1)
    gathered = []
    for first, last in chunk_bounds(half_width):
        chunk = lax.all_gather(own_half[:, first:last], "seq", axis=0, tiled=True)
        copies = [chunk]
        for shift in range(1, rep_count):
            pairs = [(j, (j + shift) % rep_count) for j in range(rep_count)]
            copies.append(lax.ppermute(chunk, "rep", pairs))
        gathered.append(copies)
    key_list = [keys]
    value_list = [values]
    clip_list = [clip_ids]
    offsets = [0]
    for distance in distances:
        below_keys, below_values, below_clips = from_behind(
            (keys, values, clip_ids), "seq", distance
        )
        above_keys, above_values, above_clips = from_behind(
            (keys, values, clip_ids), "seq", -distance
        )
        key_list += [below_keys, above_keys]
        value_list += [below_values, above_values]
        clip_list += [below_clips, above_clips]
        offsets += [distance, -distance]
    key_stack = jnp.stack(key_list)
    value_stack = jnp.stack(value_list)
    clip_stack = jnp.stack(clip_list)
    blocks = key_stack.shape[0]
    position = lax.axis_index("seq")
    window_row = lax.dynamic_index_in_dim(neighbours, position, 0, keepdims=False)
    sources = position - jnp.asarray(offsets, dtype=jnp.int32)
    present = jnp.any(
        (window_row[None, :] == sources[:, None]) & (window_row[None, :] >= 0), axis=1
    )
    key_clips = clip_stack.reshape(blocks * tile_rows)
    allowed = jnp.repeat(present, tile_rows)[None, :] & (clip_ids[:, None] == key_clips[None, :])
    key_rows = key_stack.reshape(blocks * tile_rows, feature_width)
    value_rows = value_stack.reshape(blocks * tile_rows, feature_width)
    head_outputs = []
    for head_index in range(feature_width // HD):
        first_col = head_index * HD
        head_outputs.append(
            attend_head(
                queries[:, first_col : first_col + HD],
                key_rows[:, first_col : first_col + HD],
                value_rows[:, first_col : first_col + HD],
                allowed,
            )
        )
    attended = jnp.concatenate(head_outputs, axis=1)
    head_count = lax.axis_size("head")
    head_position = lax.axis_index("head")
    received = [attended]
    for shift in range(1, head_count):
        pairs = [(j, (j + shift) % head_count) for j in range(head_count)]
        received.append(lax.ppermute(attended, "head", pairs))
    features = jnp.roll(
        jnp.concatenate(received[::-1], axis=1), (head_position + 1) * feature_width, axis=1
    )
    halves = []
    for shift in range(rep_count):
        pieces = [
            jnp.dot(features, chunk[shift], preferred_element_type=jnp.float32).astype(jnp.bfloat16)
            for chunk in gathered
        ]
        halves.append(jnp.concatenate(pieces, axis=1))
    return jnp.roll(jnp.concatenate(halves[::-1], axis=1), (rep_position + 1) * half_width, axis=1)


def solution(mesh):
    in_specs = (
        P(("rep", "seq"), "head"),
        P(("rep", "seq"), "head"),
        P(("rep", "seq"), "head"),
        P("seq", "head"),
        P("rep", None),
        P(("rep", "seq")),
    )
    out_specs = P(("rep", "seq"), "head")
    return jax.shard_map(
        on_device, mesh=mesh, in_specs=in_specs, out_specs=out_specs, check_vma=False
    )
```

```python
import math

import jax
import jax.numpy as jnp
from jax import lax
from jax.sharding import PartitionSpec as P

HD = 128
TGH = 4
TGW = 7


def from_behind(value, axis, by):
    peers = lax.axis_size(axis)
    pairs = [(i, i + by) for i in range(peers) if 0 <= i + by < peers]
    return lax.ppermute(value, axis, pairs)


def chunk_bounds(size, unit=16, parts=2):
    units = size // unit
    bounds = []
    first = 0
    for index in range(parts):
        last = size if index == parts - 1 else first + (units // parts) * unit
        if last > first:
            bounds.append((first, last))
        first = last
    return bounds


def attend_head(query_head, key_head, value_head, allowed):
    scores = lax.dot_general(
        query_head, key_head, (((1,), (1,)), ((), ())), preferred_element_type=jnp.float32
    ) * (1.0 / math.sqrt(query_head.shape[1]))
    masked = jnp.where(allowed, scores, -1e30)
    highest = jnp.max(masked, axis=1, keepdims=True)
    raised = jnp.where(allowed, jnp.exp(masked - highest), 0.0)
    summed = jnp.sum(raised, axis=1, keepdims=True)
    weights = (raised / summed).astype(jnp.bfloat16)
    return jnp.dot(weights, value_head, preferred_element_type=jnp.float32).astype(jnp.bfloat16)


def on_device(queries, keys, values, out_weight, neighbours, clip_ids):
    tile_rows = queries.shape[0]
    feature_width = queries.shape[1]
    seq_count = lax.axis_size("seq")
    layer_tiles = TGH * TGW
    every_offset = set()
    for layer_step in (-1, 0, 1):
        for row_step in (-1, 0, 1):
            for col_step in (-1, 0, 1):
                every_offset.add(layer_step * layer_tiles + row_step * TGW + col_step)
    distances = [offset for offset in sorted(every_offset) if 0 < offset < seq_count]
    rep_position = lax.axis_index("rep")
    half_width = out_weight.shape[1] // 2
    block_rows = out_weight.shape[0]
    own_half = lax.dynamic_slice_in_dim(out_weight, rep_position * half_width, half_width, axis=1)
    row_chunks = chunk_bounds(block_rows)
    gathered = [
        lax.all_gather(own_half[first:last], "seq", axis=0, tiled=True) for first, last in row_chunks
    ]
    key_list = [keys]
    value_list = [values]
    clip_list = [clip_ids]
    offsets = [0]
    for distance in distances:
        below_keys, below_values, below_clips = from_behind(
            (keys, values, clip_ids), "seq", distance
        )
        above_keys, above_values, above_clips = from_behind(
            (keys, values, clip_ids), "seq", -distance
        )
        key_list += [below_keys, above_keys]
        value_list += [below_values, above_values]
        clip_list += [below_clips, above_clips]
        offsets += [distance, -distance]
    key_stack = jnp.stack(key_list)
    value_stack = jnp.stack(value_list)
    clip_stack = jnp.stack(clip_list)
    first_chunk, key_stack, value_stack, clip_stack = lax.optimization_barrier(
        (gathered[0], key_stack, value_stack, clip_stack)
    )
    crossed = [lax.ppermute(first_chunk, "rep", [(0, 1), (1, 0)])]
    blocks = key_stack.shape[0]
    position = lax.axis_index("seq")
    window_row = lax.dynamic_index_in_dim(neighbours, position, 0, keepdims=False)
    sources = position - jnp.asarray(offsets, dtype=jnp.int32)
    present = jnp.any(
        (window_row[None, :] == sources[:, None]) & (window_row[None, :] >= 0), axis=1
    )
    key_clips = clip_stack.reshape(blocks * tile_rows)
    allowed = jnp.repeat(present, tile_rows)[None, :] & (clip_ids[:, None] == key_clips[None, :])
    key_rows = key_stack.reshape(blocks * tile_rows, feature_width)
    value_rows = value_stack.reshape(blocks * tile_rows, feature_width)
    head_outputs = []
    for head_index in range(feature_width // HD):
        first_col = head_index * HD
        head_outputs.append(
            attend_head(
                queries[:, first_col : first_col + HD],
                key_rows[:, first_col : first_col + HD],
                value_rows[:, first_col : first_col + HD],
                allowed,
            )
        )
    attended = jnp.concatenate(head_outputs, axis=1)
    attended, crossed[0] = lax.optimization_barrier((attended, crossed[0]))
    for chunk in gathered[1:]:
        crossed.append(lax.ppermute(chunk, "rep", [(0, 1), (1, 0)]))
    features = lax.all_gather(attended, "head", axis=1, tiled=True)
    blocks = features.shape[1] // block_rows
    own_sum = None
    other_sum = None
    for (first, last), chunk, twin_chunk in zip(row_chunks, gathered, crossed):
        rows = features.reshape(tile_rows, blocks, block_rows)[:, :, first:last]
        rows = rows.reshape(tile_rows, blocks * (last - first))
        own_part = jnp.dot(rows, chunk, preferred_element_type=jnp.float32)
        other_part = jnp.dot(rows, twin_chunk, preferred_element_type=jnp.float32)
        own_sum = own_part if own_sum is None else own_sum + own_part
        other_sum = other_part if other_sum is None else other_sum + other_part
    own_out = own_sum.astype(jnp.bfloat16)
    other_out = other_sum.astype(jnp.bfloat16)
    return jnp.where(
        rep_position == 0,
        jnp.concatenate([own_out, other_out], axis=1),
        jnp.concatenate([other_out, own_out], axis=1),
    )


def solution(mesh):
    in_specs = (
        P(("rep", "seq"), "head"),
        P(("rep", "seq"), "head"),
        P(("rep", "seq"), "head"),
        P("seq", "head"),
        P("rep", None),
        P(("rep", "seq")),
    )
    out_specs = P(("rep", "seq"), "head")
    return jax.shard_map(
        on_device, mesh=mesh, in_specs=in_specs, out_specs=out_specs, check_vma=False
    )
```

```python
import math

import jax
import jax.numpy as jnp
from jax import lax
from jax.sharding import PartitionSpec as P

HD = 128
TGH = 4
TGW = 7


def from_behind(value, axis, by):
    peers = lax.axis_size(axis)
    pairs = [(i, i + by) for i in range(peers) if 0 <= i + by < peers]
    return lax.ppermute(value, axis, pairs)


def chunk_bounds(size, unit=16, parts=4):
    units = size // unit
    bounds = []
    first = 0
    for index in range(parts):
        last = size if index == parts - 1 else first + (units // parts) * unit
        if last > first:
            bounds.append((first, last))
        first = last
    return bounds


def attend_head(query_head, key_head, value_head, allowed):
    scores = lax.dot_general(
        query_head, key_head, (((1,), (1,)), ((), ())), preferred_element_type=jnp.float32
    ) * (1.0 / math.sqrt(query_head.shape[1]))
    masked = jnp.where(allowed, scores, -1e30)
    highest = jnp.max(masked, axis=1, keepdims=True)
    raised = jnp.where(allowed, jnp.exp(masked - highest), 0.0)
    summed = jnp.sum(raised, axis=1, keepdims=True)
    weights = (raised / summed).astype(jnp.bfloat16)
    return jnp.dot(weights, value_head, preferred_element_type=jnp.float32).astype(jnp.bfloat16)


def on_device(queries, keys, values, out_weight, neighbours, clip_ids):
    tile_rows = queries.shape[0]
    feature_width = queries.shape[1]
    seq_count = lax.axis_size("seq")
    layer_tiles = TGH * TGW
    every_offset = set()
    for layer_step in (-1, 0, 1):
        for row_step in (-1, 0, 1):
            for col_step in (-1, 0, 1):
                every_offset.add(layer_step * layer_tiles + row_step * TGW + col_step)
    distances = [offset for offset in sorted(every_offset) if 0 < offset < seq_count]
    rep_position = lax.axis_index("rep")
    half_width = out_weight.shape[1] // 2
    block_rows = out_weight.shape[0]
    own_half = lax.dynamic_slice_in_dim(out_weight, rep_position * half_width, half_width, axis=1)
    row_chunks = chunk_bounds(block_rows)
    gathered = [
        lax.all_gather(own_half[first:last], "seq", axis=0, tiled=True) for first, last in row_chunks
    ]
    key_list = [keys]
    value_list = [values]
    clip_list = [clip_ids]
    offsets = [0]
    for distance in distances:
        below_keys, below_values, below_clips = from_behind(
            (keys, values, clip_ids), "seq", distance
        )
        above_keys, above_values, above_clips = from_behind(
            (keys, values, clip_ids), "seq", -distance
        )
        key_list += [below_keys, above_keys]
        value_list += [below_values, above_values]
        clip_list += [below_clips, above_clips]
        offsets += [distance, -distance]
    key_stack = jnp.stack(key_list)
    value_stack = jnp.stack(value_list)
    clip_stack = jnp.stack(clip_list)
    first_chunk, key_stack, value_stack, clip_stack = lax.optimization_barrier(
        (gathered[0], key_stack, value_stack, clip_stack)
    )
    crossed = [lax.ppermute(first_chunk, "rep", [(0, 1), (1, 0)])]
    blocks = key_stack.shape[0]
    position = lax.axis_index("seq")
    window_row = lax.dynamic_index_in_dim(neighbours, position, 0, keepdims=False)
    sources = position - jnp.asarray(offsets, dtype=jnp.int32)
    present = jnp.any(
        (window_row[None, :] == sources[:, None]) & (window_row[None, :] >= 0), axis=1
    )
    key_clips = clip_stack.reshape(blocks * tile_rows)
    allowed = jnp.repeat(present, tile_rows)[None, :] & (clip_ids[:, None] == key_clips[None, :])
    key_rows = key_stack.reshape(blocks * tile_rows, feature_width)
    value_rows = value_stack.reshape(blocks * tile_rows, feature_width)
    head_outputs = []
    for head_index in range(feature_width // HD):
        first_col = head_index * HD
        head_outputs.append(
            attend_head(
                queries[:, first_col : first_col + HD],
                key_rows[:, first_col : first_col + HD],
                value_rows[:, first_col : first_col + HD],
                allowed,
            )
        )
    attended = jnp.concatenate(head_outputs, axis=1)
    for index in range(1, len(gathered)):
        gathered[index], crossed[-1] = lax.optimization_barrier((gathered[index], crossed[-1]))
        crossed.append(lax.ppermute(gathered[index], "rep", [(0, 1), (1, 0)]))
    head_count = lax.axis_size("head")
    head_position = lax.axis_index("head")
    received = [attended]
    for shift in range(1, head_count):
        pairs = [(j, (j + shift) % head_count) for j in range(head_count)]
        received.append(lax.ppermute(attended, "head", pairs))
    ordered = []
    for group in range(head_count):
        block = received[0]
        for shift in range(1, head_count):
            block = jnp.where((head_position - shift) % head_count == group, received[shift], block)
        ordered.append(block)
    features = jnp.concatenate(ordered, axis=1)
    blocks = features.shape[1] // block_rows
    own_sum = None
    other_sum = None
    for (first, last), chunk, twin_chunk in zip(row_chunks, gathered, crossed):
        rows = features.reshape(tile_rows, blocks, block_rows)[:, :, first:last]
        rows = rows.reshape(tile_rows, blocks * (last - first))
        own_part = jnp.dot(rows, chunk, preferred_element_type=jnp.float32)
        other_part = jnp.dot(rows, twin_chunk, preferred_element_type=jnp.float32)
        own_sum = own_part if own_sum is None else own_sum + own_part
        other_sum = other_part if other_sum is None else other_sum + other_part
    own_out = own_sum.astype(jnp.bfloat16)
    other_out = other_sum.astype(jnp.bfloat16)
    return jnp.where(
        rep_position == 0,
        jnp.concatenate([own_out, other_out], axis=1),
        jnp.concatenate([other_out, own_out], axis=1),
    )


def solution(mesh):
    in_specs = (
        P(("rep", "seq"), "head"),
        P(("rep", "seq"), "head"),
        P(("rep", "seq"), "head"),
        P("seq", "head"),
        P("rep", None),
        P(("rep", "seq")),
    )
    out_specs = P(("rep", "seq"), "head")
    return jax.shard_map(
        on_device, mesh=mesh, in_specs=in_specs, out_specs=out_specs, check_vma=False
    )
```

```python
import math

import jax
import jax.numpy as jnp
from jax import lax
from jax.sharding import PartitionSpec as P

HD = 128
TGH = 4
TGW = 7


def from_behind(value, axis, by):
    peers = lax.axis_size(axis)
    pairs = [(i, i + by) for i in range(peers) if 0 <= i + by < peers]
    return lax.ppermute(value, axis, pairs)


def chunk_bounds(size, unit=16, parts=3):
    units = size // unit
    bounds = []
    first = 0
    for index in range(parts):
        last = size if index == parts - 1 else first + (units // parts) * unit
        if last > first:
            bounds.append((first, last))
        first = last
    return bounds


def attend_head(query_head, key_head, value_head, allowed):
    scores = lax.dot_general(
        query_head, key_head, (((1,), (1,)), ((), ())), preferred_element_type=jnp.float32
    ) * (1.0 / math.sqrt(query_head.shape[1]))
    masked = jnp.where(allowed, scores, -1e30)
    highest = jnp.max(masked, axis=1, keepdims=True)
    raised = jnp.where(allowed, jnp.exp(masked - highest), 0.0)
    summed = jnp.sum(raised, axis=1, keepdims=True)
    weights = (raised / summed).astype(jnp.bfloat16)
    return jnp.dot(weights, value_head, preferred_element_type=jnp.float32).astype(jnp.bfloat16)


def on_device(queries, keys, values, out_weight, neighbours, clip_ids):
    tile_rows = queries.shape[0]
    feature_width = queries.shape[1]
    seq_count = lax.axis_size("seq")
    layer_tiles = TGH * TGW
    every_offset = set()
    for layer_step in (-1, 0, 1):
        for row_step in (-1, 0, 1):
            for col_step in (-1, 0, 1):
                every_offset.add(layer_step * layer_tiles + row_step * TGW + col_step)
    distances = [offset for offset in sorted(every_offset) if 0 < offset < seq_count]
    rep_position = lax.axis_index("rep")
    half_width = out_weight.shape[1] // 2
    block_rows = out_weight.shape[0]
    own_half = lax.dynamic_slice_in_dim(out_weight, rep_position * half_width, half_width, axis=1)
    row_chunks = chunk_bounds(block_rows)
    gathered = [
        lax.all_gather(own_half[first:last], "seq", axis=0, tiled=True) for first, last in row_chunks
    ]
    key_list = [keys]
    value_list = [values]
    clip_list = [clip_ids]
    offsets = [0]
    for distance in distances:
        below_keys, below_values, below_clips = from_behind(
            (keys, values, clip_ids), "seq", distance
        )
        above_keys, above_values, above_clips = from_behind(
            (keys, values, clip_ids), "seq", -distance
        )
        key_list += [below_keys, above_keys]
        value_list += [below_values, above_values]
        clip_list += [below_clips, above_clips]
        offsets += [distance, -distance]
    key_stack = jnp.stack(key_list)
    value_stack = jnp.stack(value_list)
    clip_stack = jnp.stack(clip_list)
    first_chunk, key_stack, value_stack, clip_stack = lax.optimization_barrier(
        (gathered[0], key_stack, value_stack, clip_stack)
    )
    crossed = [lax.ppermute(first_chunk, "rep", [(0, 1), (1, 0)])]
    blocks = key_stack.shape[0]
    position = lax.axis_index("seq")
    window_row = lax.dynamic_index_in_dim(neighbours, position, 0, keepdims=False)
    sources = position - jnp.asarray(offsets, dtype=jnp.int32)
    present = jnp.any(
        (window_row[None, :] == sources[:, None]) & (window_row[None, :] >= 0), axis=1
    )
    key_clips = clip_stack.reshape(blocks * tile_rows)
    allowed = jnp.repeat(present, tile_rows)[None, :] & (clip_ids[:, None] == key_clips[None, :])
    key_rows = key_stack.reshape(blocks * tile_rows, feature_width)
    value_rows = value_stack.reshape(blocks * tile_rows, feature_width)
    head_outputs = []
    for head_index in range(feature_width // HD):
        first_col = head_index * HD
        head_outputs.append(
            attend_head(
                queries[:, first_col : first_col + HD],
                key_rows[:, first_col : first_col + HD],
                value_rows[:, first_col : first_col + HD],
                allowed,
            )
        )
    attended = jnp.concatenate(head_outputs, axis=1)
    for index in range(1, len(gathered)):
        gathered[index], crossed[-1] = lax.optimization_barrier((gathered[index], crossed[-1]))
        crossed.append(lax.ppermute(gathered[index], "rep", [(0, 1), (1, 0)]))
    head_count = lax.axis_size("head")
    head_position = lax.axis_index("head")
    received = [attended]
    for shift in range(1, head_count):
        pairs = [(j, (j + shift) % head_count) for j in range(head_count)]
        received.append(lax.ppermute(attended, "head", pairs))
    ordered = []
    for group in range(head_count):
        block = received[0]
        for shift in range(1, head_count):
            block = jnp.where((head_position - shift) % head_count == group, received[shift], block)
        ordered.append(block)
    features = jnp.concatenate(ordered, axis=1)
    blocks = features.shape[1] // block_rows
    own_sum = None
    other_sum = None
    for (first, last), chunk, twin_chunk in zip(row_chunks, gathered, crossed):
        rows = features.reshape(tile_rows, blocks, block_rows)[:, :, first:last]
        rows = rows.reshape(tile_rows, blocks * (last - first))
        own_part = jnp.dot(rows, chunk, preferred_element_type=jnp.float32)
        other_part = jnp.dot(rows, twin_chunk, preferred_element_type=jnp.float32)
        own_sum = own_part if own_sum is None else own_sum + own_part
        other_sum = other_part if other_sum is None else other_sum + other_part
    own_out = own_sum.astype(jnp.bfloat16)
    other_out = other_sum.astype(jnp.bfloat16)
    return jnp.where(
        rep_position == 0,
        jnp.concatenate([own_out, other_out], axis=1),
        jnp.concatenate([other_out, own_out], axis=1),
    )


def solution(mesh):
    in_specs = (
        P(("rep", "seq"), "head"),
        P(("rep", "seq"), "head"),
        P(("rep", "seq"), "head"),
        P("seq", "head"),
        P("rep", None),
        P(("rep", "seq")),
    )
    out_specs = P(("rep", "seq"), "head")
    return jax.shard_map(
        on_device, mesh=mesh, in_specs=in_specs, out_specs=out_specs, check_vma=False
    )
```

```python
import math

import jax
import jax.numpy as jnp
from jax import lax
from jax.sharding import PartitionSpec as P

HD = 128
TGH = 4
TGW = 7
LINE_LIMIT = 4


def from_behind(value, axis, by):
    peers = lax.axis_size(axis)
    pairs = [(i, i + by) for i in range(peers) if 0 <= i + by < peers]
    return lax.ppermute(value, axis, pairs)


def to_twin(value, seq_count, valid_positions):
    pairs = []
    for rep_index in (0, 1):
        for seq_index in valid_positions:
            pairs.append((rep_index * seq_count + seq_index, (1 - rep_index) * seq_count + seq_index))
    return lax.ppermute(value, ("rep", "seq"), pairs)


def attend_head(query_head, key_head, value_head, allowed):
    scores = lax.dot_general(
        query_head, key_head, (((1,), (1,)), ((), ())), preferred_element_type=jnp.float32
    ) * (1.0 / math.sqrt(query_head.shape[1]))
    masked = jnp.where(allowed, scores, -1e30)
    highest = jnp.max(masked, axis=1, keepdims=True)
    raised = jnp.where(allowed, jnp.exp(masked - highest), 0.0)
    summed = jnp.sum(raised, axis=1, keepdims=True)
    weights = (raised / summed).astype(jnp.bfloat16)
    return jnp.dot(weights, value_head, preferred_element_type=jnp.float32).astype(jnp.bfloat16)


def exchange_heads(attended):
    head_count = lax.axis_size("head")
    head_position = lax.axis_index("head")
    received = [attended]
    for shift in range(1, head_count):
        pairs = [(j, (j + shift) % head_count) for j in range(head_count)]
        received.append(lax.ppermute(attended, "head", pairs))
    ordered = []
    for group in range(head_count):
        block = received[0]
        for shift in range(1, head_count):
            block = jnp.where((head_position - shift) % head_count == group, received[shift], block)
        ordered.append(block)
    return jnp.concatenate(ordered, axis=1)


def on_device(queries, keys, values, out_weight, neighbours, clip_ids):
    tile_rows = queries.shape[0]
    feature_width = queries.shape[1]
    seq_count = lax.axis_size("seq")
    position = lax.axis_index("seq")
    rep_position = lax.axis_index("rep")
    block_rows = out_weight.shape[0]
    line_path = seq_count <= LINE_LIMIT and lax.axis_size("rep") == 2
    layer_tiles = TGH * TGW
    every_offset = set()
    for layer_step in (-1, 0, 1):
        for row_step in (-1, 0, 1):
            for col_step in (-1, 0, 1):
                every_offset.add(layer_step * layer_tiles + row_step * TGW + col_step)
    distances = [offset for offset in sorted(every_offset) if 0 < offset < seq_count]

    if line_path:
        half_width = out_weight.shape[1] // 2
        own_half = lax.dynamic_slice_in_dim(out_weight, rep_position * half_width, half_width, axis=1)
        other_half = lax.dynamic_slice_in_dim(
            out_weight, (1 - rep_position) * half_width, half_width, axis=1
        )
        from_left = from_behind(own_half, "seq", 1)
        from_right = from_behind(own_half, "seq", -1)
    else:
        weight_piece = lax.all_gather(out_weight, "seq", axis=0, tiled=True)

    key_list = [keys]
    value_list = [values]
    clip_list = [clip_ids]
    offsets = [0]
    for distance in distances:
        below_keys, below_values, below_clips = from_behind(
            (keys, values, clip_ids), "seq", distance
        )
        above_keys, above_values, above_clips = from_behind(
            (keys, values, clip_ids), "seq", -distance
        )
        key_list += [below_keys, above_keys]
        value_list += [below_values, above_values]
        clip_list += [below_clips, above_clips]
        offsets += [distance, -distance]
    key_stack = jnp.stack(key_list)
    value_stack = jnp.stack(value_list)
    clip_stack = jnp.stack(clip_list)

    arrivals = []
    if line_path:
        from_left, from_right, key_stack, value_stack, clip_stack = lax.optimization_barrier(
            (from_left, from_right, key_stack, value_stack, clip_stack)
        )
        arrivals.append((-1, from_left, to_twin(from_left, seq_count, range(1, seq_count))))
        arrivals.append((1, from_right, to_twin(from_right, seq_count, range(seq_count - 1))))

    blocks = key_stack.shape[0]
    window_row = lax.dynamic_index_in_dim(neighbours, position, 0, keepdims=False)
    sources = position - jnp.asarray(offsets, dtype=jnp.int32)
    present = jnp.any(
        (window_row[None, :] == sources[:, None]) & (window_row[None, :] >= 0), axis=1
    )
    key_clips = clip_stack.reshape(blocks * tile_rows)
    allowed = jnp.repeat(present, tile_rows)[None, :] & (clip_ids[:, None] == key_clips[None, :])
    key_rows = key_stack.reshape(blocks * tile_rows, feature_width)
    value_rows = value_stack.reshape(blocks * tile_rows, feature_width)
    head_outputs = []
    for head_index in range(feature_width // HD):
        first_col = head_index * HD
        head_outputs.append(
            attend_head(
                queries[:, first_col : first_col + HD],
                key_rows[:, first_col : first_col + HD],
                value_rows[:, first_col : first_col + HD],
                allowed,
            )
        )
    attended = jnp.concatenate(head_outputs, axis=1)

    if not line_path:
        features = exchange_heads(attended)
        projected = jnp.dot(
            lax.slice_in_dim(features, 0, weight_piece.shape[0], axis=1),
            weight_piece,
            preferred_element_type=jnp.float32,
        )
        return projected.astype(jnp.bfloat16)

    for step in range(2, seq_count):
        from_left = from_behind(from_left, "seq", 1)
        from_right = from_behind(from_right, "seq", -1)
        if step == seq_count - 1:
            twins = [twin for _, _, twin in arrivals]
            from_left, from_right, attended, twins = lax.optimization_barrier(
                (from_left, from_right, attended, twins)
            )
            arrivals = [(a, b, twin) for (a, b, _), twin in zip(arrivals, twins)]
        else:
            from_left, from_right, attended = lax.optimization_barrier(
                (from_left, from_right, attended)
            )
        arrivals.append((-step, from_left, to_twin(from_left, seq_count, range(step, seq_count))))
        arrivals.append(
            (step, from_right, to_twin(from_right, seq_count, range(seq_count - step)))
        )

    features = exchange_heads(attended)
    own_rows = lax.dynamic_slice_in_dim(features, position * block_rows, block_rows, axis=1)
    own_sum = jnp.dot(own_rows, own_half, preferred_element_type=jnp.float32)
    other_sum = jnp.dot(own_rows, other_half, preferred_element_type=jnp.float32)
    for step, own_block, twin_block in arrivals:
        source = jnp.clip(position + step, 0, seq_count - 1)
        rows = lax.dynamic_slice_in_dim(features, source * block_rows, block_rows, axis=1)
        own_sum = own_sum + jnp.dot(rows, own_block, preferred_element_type=jnp.float32)
        other_sum = other_sum + jnp.dot(rows, twin_block, preferred_element_type=jnp.float32)
    own_out = own_sum.astype(jnp.bfloat16)
    other_out = other_sum.astype(jnp.bfloat16)
    return jnp.where(
        rep_position == 0,
        jnp.concatenate([own_out, other_out], axis=1),
        jnp.concatenate([other_out, own_out], axis=1),
    )


def solution(mesh):
    in_specs = (
        P(("rep", "seq"), "head"),
        P(("rep", "seq"), "head"),
        P(("rep", "seq"), "head"),
        P("seq", "head"),
        P("rep", None),
        P(("rep", "seq")),
    )
    out_specs = P(("rep", "seq"), "head")
    return jax.shard_map(
        on_device, mesh=mesh, in_specs=in_specs, out_specs=out_specs, check_vma=False
    )
```

```python
import math

import jax
import jax.numpy as jnp
from jax import lax
from jax.sharding import PartitionSpec as P

HD = 128
TGH = 4
TGW = 7


def from_behind(value, axis, by):
    peers = lax.axis_size(axis)
    pairs = [(i, i + by) for i in range(peers) if 0 <= i + by < peers]
    return lax.ppermute(value, axis, pairs)


def attend_head(query_head, key_head, value_head, allowed):
    scores = lax.dot_general(
        query_head, key_head, (((1,), (1,)), ((), ())), preferred_element_type=jnp.float32
    ) * (1.0 / math.sqrt(query_head.shape[1]))
    masked = jnp.where(allowed, scores, -1e30)
    highest = jnp.max(masked, axis=1, keepdims=True)
    raised = jnp.where(allowed, jnp.exp(masked - highest), 0.0)
    summed = jnp.sum(raised, axis=1, keepdims=True)
    weights = (raised / summed).astype(jnp.bfloat16)
    return jnp.dot(weights, value_head, preferred_element_type=jnp.float32).astype(jnp.bfloat16)


def exchange_heads(attended):
    head_count = lax.axis_size("head")
    head_position = lax.axis_index("head")
    received = [attended]
    for shift in range(1, head_count):
        pairs = [(j, (j + shift) % head_count) for j in range(head_count)]
        received.append(lax.ppermute(attended, "head", pairs))
    ordered = []
    for group in range(head_count):
        block = received[0]
        for shift in range(1, head_count):
            block = jnp.where((head_position - shift) % head_count == group, received[shift], block)
        ordered.append(block)
    return jnp.concatenate(ordered, axis=1)


def on_device(queries, keys, values, out_weight, neighbours, clip_ids):
    tile_rows = queries.shape[0]
    feature_width = queries.shape[1]
    seq_count = lax.axis_size("seq")
    position = lax.axis_index("seq")
    rep_position = lax.axis_index("rep")
    layer_tiles = TGH * TGW
    every_offset = set()
    for layer_step in (-1, 0, 1):
        for row_step in (-1, 0, 1):
            for col_step in (-1, 0, 1):
                every_offset.add(layer_step * layer_tiles + row_step * TGW + col_step)
    distances = [offset for offset in sorted(every_offset) if 0 < offset < seq_count]

    half_width = out_weight.shape[1] // lax.axis_size("rep")
    own_half = lax.dynamic_slice_in_dim(out_weight, rep_position * half_width, half_width, axis=1)
    both_halves = lax.all_gather(own_half, ("rep", "seq"), axis=0, tiled=True)

    key_list = [keys]
    value_list = [values]
    clip_list = [clip_ids]
    offsets = [0]
    for distance in distances:
        below_keys, below_values, below_clips = from_behind(
            (keys, values, clip_ids), "seq", distance
        )
        above_keys, above_values, above_clips = from_behind(
            (keys, values, clip_ids), "seq", -distance
        )
        key_list += [below_keys, above_keys]
        value_list += [below_values, above_values]
        clip_list += [below_clips, above_clips]
        offsets += [distance, -distance]
    key_stack = jnp.stack(key_list)
    value_stack = jnp.stack(value_list)
    clip_stack = jnp.stack(clip_list)

    blocks = key_stack.shape[0]
    window_row = lax.dynamic_index_in_dim(neighbours, position, 0, keepdims=False)
    sources = position - jnp.asarray(offsets, dtype=jnp.int32)
    present = jnp.any(
        (window_row[None, :] == sources[:, None]) & (window_row[None, :] >= 0), axis=1
    )
    key_clips = clip_stack.reshape(blocks * tile_rows)
    allowed = jnp.repeat(present, tile_rows)[None, :] & (clip_ids[:, None] == key_clips[None, :])
    key_rows = key_stack.reshape(blocks * tile_rows, feature_width)
    value_rows = value_stack.reshape(blocks * tile_rows, feature_width)
    head_outputs = []
    for head_index in range(feature_width // HD):
        first_col = head_index * HD
        head_outputs.append(
            attend_head(
                queries[:, first_col : first_col + HD],
                key_rows[:, first_col : first_col + HD],
                value_rows[:, first_col : first_col + HD],
                allowed,
            )
        )
    attended = jnp.concatenate(head_outputs, axis=1)

    features = exchange_heads(attended)
    rows = features.shape[1]
    pieces = []
    for rep_index in range(lax.axis_size("rep")):
        weight_half = lax.slice_in_dim(both_halves, rep_index * rows, (rep_index + 1) * rows, axis=0)
        pieces.append(
            jnp.dot(features, weight_half, preferred_element_type=jnp.float32).astype(jnp.bfloat16)
        )
    return jnp.concatenate(pieces, axis=1)


def solution(mesh):
    in_specs = (
        P(("rep", "seq"), "head"),
        P(("rep", "seq"), "head"),
        P(("rep", "seq"), "head"),
        P("seq", "head"),
        P("rep", None),
        P(("rep", "seq")),
    )
    out_specs = P(("rep", "seq"), "head")
    return jax.shard_map(
        on_device, mesh=mesh, in_specs=in_specs, out_specs=out_specs, check_vma=False
    )
```

```python
import math

import jax
import jax.numpy as jnp
from jax import lax
from jax.sharding import PartitionSpec as P

HD = 128
TGH = 4
TGW = 7
LINE_LIMIT = 4
SC_LANES = 2


def from_behind(value, axis, by):
    peers = lax.axis_size(axis)
    pairs = [(i, i + by) for i in range(peers) if 0 <= i + by < peers]
    return lax.ppermute(value, axis, pairs)


def to_twin(value, seq_count, valid_positions):
    pairs = []
    for rep_index in (0, 1):
        for seq_index in valid_positions:
            pairs.append((rep_index * seq_count + seq_index, (1 - rep_index) * seq_count + seq_index))
    return lax.ppermute(value, ("rep", "seq"), pairs)


def attend_head(query_head, key_head, value_head, allowed):
    scores = lax.dot_general(
        query_head, key_head, (((1,), (1,)), ((), ())), preferred_element_type=jnp.float32
    ) * (1.0 / math.sqrt(query_head.shape[1]))
    masked = jnp.where(allowed, scores, -1e30)
    highest = jnp.max(masked, axis=1, keepdims=True)
    raised = jnp.where(allowed, jnp.exp(masked - highest), 0.0)
    summed = jnp.sum(raised, axis=1, keepdims=True)
    weights = (raised / summed).astype(jnp.bfloat16)
    return jnp.dot(weights, value_head, preferred_element_type=jnp.float32).astype(jnp.bfloat16)


def exchange_heads(attended):
    head_count = lax.axis_size("head")
    head_position = lax.axis_index("head")
    received = [attended]
    for shift in range(1, head_count):
        pairs = [(j, (j + shift) % head_count) for j in range(head_count)]
        received.append(lax.ppermute(attended, "head", pairs))
    ordered = []
    for group in range(head_count):
        block = received[0]
        for shift in range(1, head_count):
            block = jnp.where((head_position - shift) % head_count == group, received[shift], block)
        ordered.append(block)
    return jnp.concatenate(ordered, axis=1)


def on_device(queries, keys, values, out_weight, neighbours, clip_ids):
    tile_rows = queries.shape[0]
    feature_width = queries.shape[1]
    seq_count = lax.axis_size("seq")
    position = lax.axis_index("seq")
    rep_position = lax.axis_index("rep")
    block_rows = out_weight.shape[0]
    line_path = seq_count <= LINE_LIMIT and lax.axis_size("rep") == 2
    layer_tiles = TGH * TGW
    every_offset = set()
    for layer_step in (-1, 0, 1):
        for row_step in (-1, 0, 1):
            for col_step in (-1, 0, 1):
                every_offset.add(layer_step * layer_tiles + row_step * TGW + col_step)
    distances = [offset for offset in sorted(every_offset) if 0 < offset < seq_count]

    if line_path:
        half_width = out_weight.shape[1] // 2
        sc_width = SC_LANES * 128
        own_full = lax.dynamic_slice_in_dim(out_weight, rep_position * half_width, half_width, axis=1)
        other_full = lax.dynamic_slice_in_dim(
            out_weight, (1 - rep_position) * half_width, half_width, axis=1
        )
        both_sc = lax.all_gather(own_full[:, :sc_width], ("rep", "seq"), axis=0, tiled=True)
        own_half = own_full[:, sc_width:]
        other_half = other_full[:, sc_width:]
        from_left = from_behind(own_half, "seq", 1)
        from_right = from_behind(own_half, "seq", -1)
    else:
        weight_piece = lax.all_gather(out_weight, "seq", axis=0, tiled=True)

    key_list = [keys]
    value_list = [values]
    clip_list = [clip_ids]
    offsets = [0]
    for distance in distances:
        below_keys, below_values, below_clips = from_behind(
            (keys, values, clip_ids), "seq", distance
        )
        above_keys, above_values, above_clips = from_behind(
            (keys, values, clip_ids), "seq", -distance
        )
        key_list += [below_keys, above_keys]
        value_list += [below_values, above_values]
        clip_list += [below_clips, above_clips]
        offsets += [distance, -distance]
    key_stack = jnp.stack(key_list)
    value_stack = jnp.stack(value_list)
    clip_stack = jnp.stack(clip_list)

    arrivals = []
    if line_path:
        from_left, from_right, key_stack, value_stack, clip_stack = lax.optimization_barrier(
            (from_left, from_right, key_stack, value_stack, clip_stack)
        )
        arrivals.append((-1, from_left, to_twin(from_left, seq_count, range(1, seq_count))))
        arrivals.append((1, from_right, to_twin(from_right, seq_count, range(seq_count - 1))))

    blocks = key_stack.shape[0]
    window_row = lax.dynamic_index_in_dim(neighbours, position, 0, keepdims=False)
    sources = position - jnp.asarray(offsets, dtype=jnp.int32)
    present = jnp.any(
        (window_row[None, :] == sources[:, None]) & (window_row[None, :] >= 0), axis=1
    )
    key_clips = clip_stack.reshape(blocks * tile_rows)
    allowed = jnp.repeat(present, tile_rows)[None, :] & (clip_ids[:, None] == key_clips[None, :])
    key_rows = key_stack.reshape(blocks * tile_rows, feature_width)
    value_rows = value_stack.reshape(blocks * tile_rows, feature_width)
    head_outputs = []
    for head_index in range(feature_width // HD):
        first_col = head_index * HD
        head_outputs.append(
            attend_head(
                queries[:, first_col : first_col + HD],
                key_rows[:, first_col : first_col + HD],
                value_rows[:, first_col : first_col + HD],
                allowed,
            )
        )
    attended = jnp.concatenate(head_outputs, axis=1)

    if not line_path:
        features = exchange_heads(attended)
        projected = jnp.dot(
            lax.slice_in_dim(features, 0, weight_piece.shape[0], axis=1),
            weight_piece,
            preferred_element_type=jnp.float32,
        )
        return projected.astype(jnp.bfloat16)

    for step in range(2, seq_count):
        from_left = from_behind(from_left, "seq", 1)
        from_right = from_behind(from_right, "seq", -1)
        if step == seq_count - 1:
            twins = [twin for _, _, twin in arrivals]
            from_left, from_right, attended, twins = lax.optimization_barrier(
                (from_left, from_right, attended, twins)
            )
            arrivals = [(a, b, twin) for (a, b, _), twin in zip(arrivals, twins)]
        else:
            from_left, from_right, attended = lax.optimization_barrier(
                (from_left, from_right, attended)
            )
        arrivals.append((-step, from_left, to_twin(from_left, seq_count, range(step, seq_count))))
        arrivals.append(
            (step, from_right, to_twin(from_right, seq_count, range(seq_count - step)))
        )

    features = exchange_heads(attended)
    own_rows = lax.dynamic_slice_in_dim(features, position * block_rows, block_rows, axis=1)
    own_sum = jnp.dot(own_rows, own_half, preferred_element_type=jnp.float32)
    other_sum = jnp.dot(own_rows, other_half, preferred_element_type=jnp.float32)
    for step, own_block, twin_block in arrivals:
        source = jnp.clip(position + step, 0, seq_count - 1)
        rows = lax.dynamic_slice_in_dim(features, source * block_rows, block_rows, axis=1)
        own_sum = own_sum + jnp.dot(rows, own_block, preferred_element_type=jnp.float32)
        other_sum = other_sum + jnp.dot(rows, twin_block, preferred_element_type=jnp.float32)
    own_out = own_sum.astype(jnp.bfloat16)
    other_out = other_sum.astype(jnp.bfloat16)
    rows = features.shape[1]
    sc_parts = [
        jnp.dot(
            features,
            lax.slice_in_dim(both_sc, index * rows, (index + 1) * rows, axis=0),
            preferred_element_type=jnp.float32,
        ).astype(jnp.bfloat16)
        for index in range(2)
    ]
    first_line = jnp.where(rep_position == 0, own_out, other_out)
    second_line = jnp.where(rep_position == 0, other_out, own_out)
    return jnp.concatenate([sc_parts[0], first_line, sc_parts[1], second_line], axis=1)


def solution(mesh):
    in_specs = (
        P(("rep", "seq"), "head"),
        P(("rep", "seq"), "head"),
        P(("rep", "seq"), "head"),
        P("seq", "head"),
        P("rep", None),
        P(("rep", "seq")),
    )
    out_specs = P(("rep", "seq"), "head")
    return jax.shard_map(
        on_device, mesh=mesh, in_specs=in_specs, out_specs=out_specs, check_vma=False
    )
```

```python
import math

import jax
import jax.numpy as jnp
from jax import lax
from jax.sharding import PartitionSpec as P

HD = 128
TGH = 4
TGW = 7
LINE_LIMIT = 4
SC_LANES = 2


def from_behind(value, axis, by):
    peers = lax.axis_size(axis)
    pairs = [(i, i + by) for i in range(peers) if 0 <= i + by < peers]
    return lax.ppermute(value, axis, pairs)


def to_twin(value, seq_count, valid_positions):
    pairs = []
    for rep_index in (0, 1):
        for seq_index in valid_positions:
            pairs.append((rep_index * seq_count + seq_index, (1 - rep_index) * seq_count + seq_index))
    return lax.ppermute(value, ("rep", "seq"), pairs)


def attend_head(query_head, key_head, value_head, allowed):
    scores = lax.dot_general(
        query_head, key_head, (((1,), (1,)), ((), ())), preferred_element_type=jnp.float32
    ) * (1.0 / math.sqrt(query_head.shape[1]))
    masked = jnp.where(allowed, scores, -1e30)
    highest = jnp.max(masked, axis=1, keepdims=True)
    raised = jnp.where(allowed, jnp.exp(masked - highest), 0.0)
    summed = jnp.sum(raised, axis=1, keepdims=True)
    weights = (raised / summed).astype(jnp.bfloat16)
    return jnp.dot(weights, value_head, preferred_element_type=jnp.float32).astype(jnp.bfloat16)


def exchange_heads(attended):
    head_count = lax.axis_size("head")
    head_position = lax.axis_index("head")
    received = [attended]
    for shift in range(1, head_count):
        pairs = [(j, (j + shift) % head_count) for j in range(head_count)]
        received.append(lax.ppermute(attended, "head", pairs))
    ordered = []
    for group in range(head_count):
        block = received[0]
        for shift in range(1, head_count):
            block = jnp.where((head_position - shift) % head_count == group, received[shift], block)
        ordered.append(block)
    return jnp.concatenate(ordered, axis=1)


def on_device(queries, keys, values, out_weight, neighbours, clip_ids):
    tile_rows = queries.shape[0]
    feature_width = queries.shape[1]
    seq_count = lax.axis_size("seq")
    position = lax.axis_index("seq")
    rep_position = lax.axis_index("rep")
    block_rows = out_weight.shape[0]
    line_path = seq_count <= LINE_LIMIT and lax.axis_size("rep") == 2
    layer_tiles = TGH * TGW
    every_offset = set()
    for layer_step in (-1, 0, 1):
        for row_step in (-1, 0, 1):
            for col_step in (-1, 0, 1):
                every_offset.add(layer_step * layer_tiles + row_step * TGW + col_step)
    distances = [offset for offset in sorted(every_offset) if 0 < offset < seq_count]

    if line_path:
        half_width = out_weight.shape[1] // 2
        sc_width = SC_LANES * 128
        own_full = lax.dynamic_slice_in_dim(out_weight, rep_position * half_width, half_width, axis=1)
        other_full = lax.dynamic_slice_in_dim(
            out_weight, (1 - rep_position) * half_width, half_width, axis=1
        )
        both_sc = lax.all_gather(own_full[:, :sc_width], ("rep", "seq"), axis=0, tiled=True)
        own_half = own_full[:, sc_width:]
        other_half = other_full[:, sc_width:]
        from_left = from_behind(own_half, "seq", 1)
        from_right = from_behind(own_half, "seq", -1)
    else:
        weight_piece = lax.all_gather(out_weight, "seq", axis=0, tiled=True)

    key_list = [keys]
    value_list = [values]
    clip_list = [clip_ids]
    offsets = [0]
    for distance in distances:
        below_keys, below_values, below_clips = from_behind(
            (keys, values, clip_ids), "seq", distance
        )
        above_keys, above_values, above_clips = from_behind(
            (keys, values, clip_ids), "seq", -distance
        )
        key_list += [below_keys, above_keys]
        value_list += [below_values, above_values]
        clip_list += [below_clips, above_clips]
        offsets += [distance, -distance]
    key_stack = jnp.stack(key_list)
    value_stack = jnp.stack(value_list)
    clip_stack = jnp.stack(clip_list)

    arrivals = []
    if line_path:
        from_left, from_right, key_stack, value_stack, clip_stack, both_sc = lax.optimization_barrier(
            (from_left, from_right, key_stack, value_stack, clip_stack, both_sc)
        )
        arrivals.append((-1, from_left, to_twin(from_left, seq_count, range(1, seq_count))))
        arrivals.append((1, from_right, to_twin(from_right, seq_count, range(seq_count - 1))))

    blocks = key_stack.shape[0]
    window_row = lax.dynamic_index_in_dim(neighbours, position, 0, keepdims=False)
    sources = position - jnp.asarray(offsets, dtype=jnp.int32)
    present = jnp.any(
        (window_row[None, :] == sources[:, None]) & (window_row[None, :] >= 0), axis=1
    )
    key_clips = clip_stack.reshape(blocks * tile_rows)
    allowed = jnp.repeat(present, tile_rows)[None, :] & (clip_ids[:, None] == key_clips[None, :])
    key_rows = key_stack.reshape(blocks * tile_rows, feature_width)
    value_rows = value_stack.reshape(blocks * tile_rows, feature_width)
    head_outputs = []
    for head_index in range(feature_width // HD):
        first_col = head_index * HD
        head_outputs.append(
            attend_head(
                queries[:, first_col : first_col + HD],
                key_rows[:, first_col : first_col + HD],
                value_rows[:, first_col : first_col + HD],
                allowed,
            )
        )
    attended = jnp.concatenate(head_outputs, axis=1)

    if not line_path:
        features = exchange_heads(attended)
        projected = jnp.dot(
            lax.slice_in_dim(features, 0, weight_piece.shape[0], axis=1),
            weight_piece,
            preferred_element_type=jnp.float32,
        )
        return projected.astype(jnp.bfloat16)

    for step in range(2, seq_count):
        from_left = from_behind(from_left, "seq", 1)
        from_right = from_behind(from_right, "seq", -1)
        if step == seq_count - 1:
            twins = [twin for _, _, twin in arrivals]
            from_left, from_right, attended, twins = lax.optimization_barrier(
                (from_left, from_right, attended, twins)
            )
            arrivals = [(a, b, twin) for (a, b, _), twin in zip(arrivals, twins)]
        else:
            from_left, from_right, attended = lax.optimization_barrier(
                (from_left, from_right, attended)
            )
        arrivals.append((-step, from_left, to_twin(from_left, seq_count, range(step, seq_count))))
        arrivals.append(
            (step, from_right, to_twin(from_right, seq_count, range(seq_count - step)))
        )

    features = exchange_heads(attended)
    own_rows = lax.dynamic_slice_in_dim(features, position * block_rows, block_rows, axis=1)
    own_sum = jnp.dot(own_rows, own_half, preferred_element_type=jnp.float32)
    other_sum = jnp.dot(own_rows, other_half, preferred_element_type=jnp.float32)
    for step, own_block, twin_block in arrivals:
        source = jnp.clip(position + step, 0, seq_count - 1)
        rows = lax.dynamic_slice_in_dim(features, source * block_rows, block_rows, axis=1)
        own_sum = own_sum + jnp.dot(rows, own_block, preferred_element_type=jnp.float32)
        other_sum = other_sum + jnp.dot(rows, twin_block, preferred_element_type=jnp.float32)
    own_out = own_sum.astype(jnp.bfloat16)
    other_out = other_sum.astype(jnp.bfloat16)
    rows = features.shape[1]
    sc_parts = [
        jnp.dot(
            features,
            lax.slice_in_dim(both_sc, index * rows, (index + 1) * rows, axis=0),
            preferred_element_type=jnp.float32,
        ).astype(jnp.bfloat16)
        for index in range(2)
    ]
    first_line = jnp.where(rep_position == 0, own_out, other_out)
    second_line = jnp.where(rep_position == 0, other_out, own_out)
    return jnp.concatenate([sc_parts[0], first_line, sc_parts[1], second_line], axis=1)


def solution(mesh):
    in_specs = (
        P(("rep", "seq"), "head"),
        P(("rep", "seq"), "head"),
        P(("rep", "seq"), "head"),
        P("seq", "head"),
        P("rep", None),
        P(("rep", "seq")),
    )
    out_specs = P(("rep", "seq"), "head")
    return jax.shard_map(
        on_device, mesh=mesh, in_specs=in_specs, out_specs=out_specs, check_vma=False
    )
```

```python
import math

import jax
import jax.numpy as jnp
from jax import lax
from jax.sharding import PartitionSpec as P

HD = 128
TGH = 4
TGW = 7
LINE_LIMIT = 4


def from_behind(value, axis, by):
    peers = lax.axis_size(axis)
    pairs = [(i, i + by) for i in range(peers) if 0 <= i + by < peers]
    return lax.ppermute(value, axis, pairs)


def to_twin(value, seq_count, valid_positions):
    pairs = []
    for rep_index in (0, 1):
        for seq_index in valid_positions:
            pairs.append((rep_index * seq_count + seq_index, (1 - rep_index) * seq_count + seq_index))
    return lax.ppermute(value, ("rep", "seq"), pairs)


def attend_head(query_head, key_head, value_head, allowed):
    scores = lax.dot_general(
        query_head, key_head, (((1,), (1,)), ((), ())), preferred_element_type=jnp.float32
    ) * (1.0 / math.sqrt(query_head.shape[1]))
    masked = jnp.where(allowed, scores, -1e30)
    highest = jnp.max(masked, axis=1, keepdims=True)
    raised = jnp.where(allowed, jnp.exp(masked - highest), 0.0)
    summed = jnp.sum(raised, axis=1, keepdims=True)
    weights = (raised / summed).astype(jnp.bfloat16)
    return jnp.dot(weights, value_head, preferred_element_type=jnp.float32).astype(jnp.bfloat16)


def exchange_heads(attended):
    head_count = lax.axis_size("head")
    head_position = lax.axis_index("head")
    received = [attended]
    for shift in range(1, head_count):
        pairs = [(j, (j + shift) % head_count) for j in range(head_count)]
        received.append(lax.ppermute(attended, "head", pairs))
    ordered = []
    for group in range(head_count):
        block = received[0]
        for shift in range(1, head_count):
            block = jnp.where((head_position - shift) % head_count == group, received[shift], block)
        ordered.append(block)
    return jnp.concatenate(ordered, axis=1)


def on_device(queries, keys, values, out_weight, neighbours, clip_ids):
    tile_rows = queries.shape[0]
    feature_width = queries.shape[1]
    seq_count = lax.axis_size("seq")
    position = lax.axis_index("seq")
    rep_position = lax.axis_index("rep")
    block_rows = out_weight.shape[0]
    line_path = seq_count <= LINE_LIMIT and lax.axis_size("rep") == 2
    layer_tiles = TGH * TGW
    every_offset = set()
    for layer_step in (-1, 0, 1):
        for row_step in (-1, 0, 1):
            for col_step in (-1, 0, 1):
                every_offset.add(layer_step * layer_tiles + row_step * TGW + col_step)
    distances = [offset for offset in sorted(every_offset) if 0 < offset < seq_count]

    if line_path:
        half_width = out_weight.shape[1] // 2
        own_half = lax.dynamic_slice_in_dim(out_weight, rep_position * half_width, half_width, axis=1)
        other_half = lax.dynamic_slice_in_dim(
            out_weight, (1 - rep_position) * half_width, half_width, axis=1
        )
        from_left = from_behind(own_half, "seq", 1)
        from_right = from_behind(own_half, "seq", -1)
    else:
        weight_piece = lax.all_gather(out_weight, "seq", axis=0, tiled=True)

    key_list = [keys]
    value_list = [values]
    clip_list = [clip_ids]
    offsets = [0]
    for distance in distances:
        below_keys, below_values, below_clips = from_behind(
            (keys, values, clip_ids), "seq", distance
        )
        above_keys, above_values, above_clips = from_behind(
            (keys, values, clip_ids), "seq", -distance
        )
        key_list += [below_keys, above_keys]
        value_list += [below_values, above_values]
        clip_list += [below_clips, above_clips]
        offsets += [distance, -distance]
    key_stack = jnp.stack(key_list)
    value_stack = jnp.stack(value_list)
    clip_stack = jnp.stack(clip_list)

    arrivals = []
    if line_path:
        from_left, from_right, key_stack, value_stack, clip_stack = lax.optimization_barrier(
            (from_left, from_right, key_stack, value_stack, clip_stack)
        )
        arrivals.append((-1, from_left, to_twin(from_left, seq_count, range(1, seq_count))))
        arrivals.append((1, from_right, to_twin(from_right, seq_count, range(seq_count - 1))))

    blocks = key_stack.shape[0]
    window_row = lax.dynamic_index_in_dim(neighbours, position, 0, keepdims=False)
    sources = position - jnp.asarray(offsets, dtype=jnp.int32)
    present = jnp.any(
        (window_row[None, :] == sources[:, None]) & (window_row[None, :] >= 0), axis=1
    )
    key_clips = clip_stack.reshape(blocks * tile_rows)
    allowed = jnp.repeat(present, tile_rows)[None, :] & (clip_ids[:, None] == key_clips[None, :])
    key_rows = key_stack.reshape(blocks * tile_rows, feature_width)
    value_rows = value_stack.reshape(blocks * tile_rows, feature_width)
    head_outputs = []
    for head_index in range(feature_width // HD):
        first_col = head_index * HD
        head_outputs.append(
            attend_head(
                queries[:, first_col : first_col + HD],
                key_rows[:, first_col : first_col + HD],
                value_rows[:, first_col : first_col + HD],
                allowed,
            )
        )
    attended = jnp.concatenate(head_outputs, axis=1)

    if not line_path:
        features = exchange_heads(attended)
        projected = jnp.dot(
            lax.slice_in_dim(features, 0, weight_piece.shape[0], axis=1),
            weight_piece,
            preferred_element_type=jnp.float32,
        )
        return projected.astype(jnp.bfloat16)

    for step in range(2, seq_count):
        from_left = from_behind(from_left, "seq", 1)
        from_right = from_behind(from_right, "seq", -1)
        earlier = [arrivals[-2][2], arrivals[-1][2]]
        if step == 2:
            from_left, from_right, attended, earlier = lax.optimization_barrier(
                (from_left, from_right, attended, earlier)
            )
        else:
            from_left, from_right, earlier = lax.optimization_barrier(
                (from_left, from_right, earlier)
            )
        arrivals[-2] = arrivals[-2][:2] + (earlier[0],)
        arrivals[-1] = arrivals[-1][:2] + (earlier[1],)
        arrivals.append((-step, from_left, to_twin(from_left, seq_count, range(step, seq_count))))
        arrivals.append(
            (step, from_right, to_twin(from_right, seq_count, range(seq_count - step)))
        )

    features = exchange_heads(attended)
    own_rows = lax.dynamic_slice_in_dim(features, position * block_rows, block_rows, axis=1)
    own_sum = jnp.dot(own_rows, own_half, preferred_element_type=jnp.float32)
    other_sum = jnp.dot(own_rows, other_half, preferred_element_type=jnp.float32)
    for step, own_block, twin_block in arrivals:
        source = jnp.clip(position + step, 0, seq_count - 1)
        rows = lax.dynamic_slice_in_dim(features, source * block_rows, block_rows, axis=1)
        own_sum = own_sum + jnp.dot(rows, own_block, preferred_element_type=jnp.float32)
        other_sum = other_sum + jnp.dot(rows, twin_block, preferred_element_type=jnp.float32)
    own_out = own_sum.astype(jnp.bfloat16)
    other_out = other_sum.astype(jnp.bfloat16)
    return jnp.where(
        rep_position == 0,
        jnp.concatenate([own_out, other_out], axis=1),
        jnp.concatenate([other_out, own_out], axis=1),
    )


def solution(mesh):
    in_specs = (
        P(("rep", "seq"), "head"),
        P(("rep", "seq"), "head"),
        P(("rep", "seq"), "head"),
        P("seq", "head"),
        P("rep", None),
        P(("rep", "seq")),
    )
    out_specs = P(("rep", "seq"), "head")
    return jax.shard_map(
        on_device, mesh=mesh, in_specs=in_specs, out_specs=out_specs, check_vma=False
    )
```

```python
import math

import jax
import jax.numpy as jnp
from jax import lax
from jax.sharding import PartitionSpec as P

HD = 128
TGH = 4
TGW = 7


def from_behind(value, axis, by):
    peers = lax.axis_size(axis)
    pairs = [(i, i + by) for i in range(peers) if 0 <= i + by < peers]
    return lax.ppermute(value, axis, pairs)


def attend_head(query_head, key_head, value_head, allowed):
    scores = lax.dot_general(
        query_head, key_head, (((1,), (1,)), ((), ())), preferred_element_type=jnp.float32
    ) * (1.0 / math.sqrt(query_head.shape[1]))
    masked = jnp.where(allowed, scores, -1e30)
    highest = jnp.max(masked, axis=1, keepdims=True)
    raised = jnp.where(allowed, jnp.exp(masked - highest), 0.0)
    summed = jnp.sum(raised, axis=1, keepdims=True)
    weights = (raised / summed).astype(jnp.bfloat16)
    return jnp.dot(weights, value_head, preferred_element_type=jnp.float32).astype(jnp.bfloat16)


def exchange_heads(attended):
    head_count = lax.axis_size("head")
    head_position = lax.axis_index("head")
    received = [attended]
    for shift in range(1, head_count):
        pairs = [(j, (j + shift) % head_count) for j in range(head_count)]
        received.append(lax.ppermute(attended, "head", pairs))
    ordered = []
    for group in range(head_count):
        block = received[0]
        for shift in range(1, head_count):
            block = jnp.where((head_position - shift) % head_count == group, received[shift], block)
        ordered.append(block)
    return jnp.concatenate(ordered, axis=1)


def on_device(queries, keys, values, out_weight, neighbours, clip_ids):
    tile_rows = queries.shape[0]
    feature_width = queries.shape[1]
    seq_count = lax.axis_size("seq")
    position = lax.axis_index("seq")
    rep_position = lax.axis_index("rep")
    layer_tiles = TGH * TGW
    every_offset = set()
    for layer_step in (-1, 0, 1):
        for row_step in (-1, 0, 1):
            for col_step in (-1, 0, 1):
                every_offset.add(layer_step * layer_tiles + row_step * TGW + col_step)
    distances = [offset for offset in sorted(every_offset) if 0 < offset < seq_count]

    rep_count = lax.axis_size("rep")
    part_rows = out_weight.shape[0] // rep_count
    own_part = lax.dynamic_slice_in_dim(out_weight, rep_position * part_rows, part_rows, axis=0)
    both_parts = lax.all_gather(own_part, ("rep", "seq"), axis=0, tiled=True)

    key_list = [keys]
    value_list = [values]
    clip_list = [clip_ids]
    offsets = [0]
    for distance in distances:
        below_keys, below_values, below_clips = from_behind(
            (keys, values, clip_ids), "seq", distance
        )
        above_keys, above_values, above_clips = from_behind(
            (keys, values, clip_ids), "seq", -distance
        )
        key_list += [below_keys, above_keys]
        value_list += [below_values, above_values]
        clip_list += [below_clips, above_clips]
        offsets += [distance, -distance]
    key_stack = jnp.stack(key_list)
    value_stack = jnp.stack(value_list)
    clip_stack = jnp.stack(clip_list)

    blocks = key_stack.shape[0]
    window_row = lax.dynamic_index_in_dim(neighbours, position, 0, keepdims=False)
    sources = position - jnp.asarray(offsets, dtype=jnp.int32)
    present = jnp.any(
        (window_row[None, :] == sources[:, None]) & (window_row[None, :] >= 0), axis=1
    )
    key_clips = clip_stack.reshape(blocks * tile_rows)
    allowed = jnp.repeat(present, tile_rows)[None, :] & (clip_ids[:, None] == key_clips[None, :])
    key_rows = key_stack.reshape(blocks * tile_rows, feature_width)
    value_rows = value_stack.reshape(blocks * tile_rows, feature_width)
    head_outputs = []
    for head_index in range(feature_width // HD):
        first_col = head_index * HD
        head_outputs.append(
            attend_head(
                queries[:, first_col : first_col + HD],
                key_rows[:, first_col : first_col + HD],
                value_rows[:, first_col : first_col + HD],
                allowed,
            )
        )
    attended = jnp.concatenate(head_outputs, axis=1)

    features = exchange_heads(attended)
    regrouped = features.reshape(tile_rows, seq_count, rep_count, part_rows)
    regrouped = jnp.swapaxes(regrouped, 1, 2).reshape(tile_rows, features.shape[1])
    projected = jnp.dot(regrouped, both_parts, preferred_element_type=jnp.float32)
    return projected.astype(jnp.bfloat16)


def solution(mesh):
    in_specs = (
        P(("rep", "seq"), "head"),
        P(("rep", "seq"), "head"),
        P(("rep", "seq"), "head"),
        P("seq", "head"),
        P("rep", None),
        P(("rep", "seq")),
    )
    out_specs = P(("rep", "seq"), "head")
    return jax.shard_map(
        on_device, mesh=mesh, in_specs=in_specs, out_specs=out_specs, check_vma=False
    )
```

```python
import math

import jax
import jax.numpy as jnp
from jax import lax
from jax.sharding import PartitionSpec as P

HD = 128
TGH = 4
TGW = 7


def from_behind(value, axis, by):
    peers = lax.axis_size(axis)
    pairs = [(i, i + by) for i in range(peers) if 0 <= i + by < peers]
    return lax.ppermute(value, axis, pairs)


def attend_head(query_head, key_head, value_head, allowed):
    scores = lax.dot_general(
        query_head, key_head, (((1,), (1,)), ((), ())), preferred_element_type=jnp.float32
    ) * (1.0 / math.sqrt(query_head.shape[1]))
    masked = jnp.where(allowed, scores, -1e30)
    highest = jnp.max(masked, axis=1, keepdims=True)
    raised = jnp.where(allowed, jnp.exp(masked - highest), 0.0)
    summed = jnp.sum(raised, axis=1, keepdims=True)
    weights = (raised / summed).astype(jnp.bfloat16)
    return jnp.dot(weights, value_head, preferred_element_type=jnp.float32).astype(jnp.bfloat16)


def exchange_heads(attended):
    head_count = lax.axis_size("head")
    head_position = lax.axis_index("head")
    received = [attended]
    for shift in range(1, head_count):
        pairs = [(j, (j + shift) % head_count) for j in range(head_count)]
        received.append(lax.ppermute(attended, "head", pairs))
    ordered = []
    for group in range(head_count):
        block = received[0]
        for shift in range(1, head_count):
            block = jnp.where((head_position - shift) % head_count == group, received[shift], block)
        ordered.append(block)
    return jnp.concatenate(ordered, axis=1)


def on_device(queries, keys, values, out_weight, neighbours, clip_ids):
    tile_rows = queries.shape[0]
    feature_width = queries.shape[1]
    seq_count = lax.axis_size("seq")
    position = lax.axis_index("seq")
    rep_position = lax.axis_index("rep")
    layer_tiles = TGH * TGW
    every_offset = set()
    for layer_step in (-1, 0, 1):
        for row_step in (-1, 0, 1):
            for col_step in (-1, 0, 1):
                every_offset.add(layer_step * layer_tiles + row_step * TGW + col_step)
    distances = [offset for offset in sorted(every_offset) if 0 < offset < seq_count]

    rep_count = lax.axis_size("rep")
    part_rows = out_weight.shape[0] // rep_count
    own_part = lax.dynamic_slice_in_dim(out_weight, rep_position * part_rows, part_rows, axis=0)
    both_parts = lax.all_gather(own_part, ("rep", "seq"), axis=0, tiled=True)

    key_list = [keys]
    value_list = [values]
    clip_list = [clip_ids]
    offsets = [0]
    joined = jnp.concatenate([keys, values], axis=1)
    for distance in distances:
        for signed in (distance, -distance):
            moved = from_behind(joined, "seq", signed)
            key_list.append(moved[:, :feature_width])
            value_list.append(moved[:, feature_width:])
            clip_list.append(from_behind(clip_ids, "seq", signed))
            offsets.append(signed)
    key_stack = jnp.stack(key_list)
    value_stack = jnp.stack(value_list)
    clip_stack = jnp.stack(clip_list)

    blocks = key_stack.shape[0]
    window_row = lax.dynamic_index_in_dim(neighbours, position, 0, keepdims=False)
    sources = position - jnp.asarray(offsets, dtype=jnp.int32)
    present = jnp.any(
        (window_row[None, :] == sources[:, None]) & (window_row[None, :] >= 0), axis=1
    )
    key_clips = clip_stack.reshape(blocks * tile_rows)
    allowed = jnp.repeat(present, tile_rows)[None, :] & (clip_ids[:, None] == key_clips[None, :])
    key_rows = key_stack.reshape(blocks * tile_rows, feature_width)
    value_rows = value_stack.reshape(blocks * tile_rows, feature_width)
    head_outputs = []
    for head_index in range(feature_width // HD):
        first_col = head_index * HD
        head_outputs.append(
            attend_head(
                queries[:, first_col : first_col + HD],
                key_rows[:, first_col : first_col + HD],
                value_rows[:, first_col : first_col + HD],
                allowed,
            )
        )
    attended = jnp.concatenate(head_outputs, axis=1)

    features = exchange_heads(attended)
    regrouped = features.reshape(tile_rows, seq_count, rep_count, part_rows)
    regrouped = jnp.swapaxes(regrouped, 1, 2).reshape(tile_rows, features.shape[1])
    projected = jnp.dot(regrouped, both_parts, preferred_element_type=jnp.float32)
    return projected.astype(jnp.bfloat16)


def solution(mesh):
    in_specs = (
        P(("rep", "seq"), "head"),
        P(("rep", "seq"), "head"),
        P(("rep", "seq"), "head"),
        P("seq", "head"),
        P("rep", None),
        P(("rep", "seq")),
    )
    out_specs = P(("rep", "seq"), "head")
    return jax.shard_map(
        on_device, mesh=mesh, in_specs=in_specs, out_specs=out_specs, check_vma=False
    )
```

```python
import math

import jax
import jax.numpy as jnp
from jax import lax
from jax.sharding import PartitionSpec as P

HD = 128
TGH = 4
TGW = 7


def from_behind(value, axis, by):
    peers = lax.axis_size(axis)
    pairs = [(i, i + by) for i in range(peers) if 0 <= i + by < peers]
    return lax.ppermute(value, axis, pairs)


def attend_head(query_head, key_head, value_head, allowed):
    scores = lax.dot_general(
        query_head, key_head, (((1,), (1,)), ((), ())), preferred_element_type=jnp.float32
    ) * (1.0 / math.sqrt(query_head.shape[1]))
    masked = jnp.where(allowed, scores, -1e30)
    highest = jnp.max(masked, axis=1, keepdims=True)
    raised = jnp.where(allowed, jnp.exp(masked - highest), 0.0)
    summed = jnp.sum(raised, axis=1, keepdims=True)
    weights = (raised / summed).astype(jnp.bfloat16)
    return jnp.dot(weights, value_head, preferred_element_type=jnp.float32).astype(jnp.bfloat16)


def exchange_heads(attended):
    head_count = lax.axis_size("head")
    head_position = lax.axis_index("head")
    received = [attended]
    for shift in range(1, head_count):
        pairs = [(j, (j + shift) % head_count) for j in range(head_count)]
        received.append(lax.ppermute(attended, "head", pairs))
    ordered = []
    for group in range(head_count):
        block = received[0]
        for shift in range(1, head_count):
            block = jnp.where((head_position - shift) % head_count == group, received[shift], block)
        ordered.append(block)
    return jnp.concatenate(ordered, axis=1)


def on_device(queries, keys, values, out_weight, neighbours, clip_ids):
    tile_rows = queries.shape[0]
    feature_width = queries.shape[1]
    seq_count = lax.axis_size("seq")
    position = lax.axis_index("seq")
    rep_position = lax.axis_index("rep")
    layer_tiles = TGH * TGW
    every_offset = set()
    for layer_step in (-1, 0, 1):
        for row_step in (-1, 0, 1):
            for col_step in (-1, 0, 1):
                every_offset.add(layer_step * layer_tiles + row_step * TGW + col_step)
    distances = [offset for offset in sorted(every_offset) if 0 < offset < seq_count]

    rep_count = lax.axis_size("rep")
    part_rows = out_weight.shape[0] // rep_count
    own_part = out_weight[:part_rows]
    for rep_index in range(1, rep_count):
        own_part = jnp.where(
            rep_position == rep_index,
            out_weight[rep_index * part_rows : (rep_index + 1) * part_rows],
            own_part,
        )
    both_parts = lax.all_gather(own_part, ("rep", "seq"), axis=0, tiled=True)

    key_list = [keys]
    value_list = [values]
    clip_list = [clip_ids]
    offsets = [0]
    for distance in distances:
        below_keys, below_values, below_clips = from_behind(
            (keys, values, clip_ids), "seq", distance
        )
        above_keys, above_values, above_clips = from_behind(
            (keys, values, clip_ids), "seq", -distance
        )
        key_list += [below_keys, above_keys]
        value_list += [below_values, above_values]
        clip_list += [below_clips, above_clips]
        offsets += [distance, -distance]
    key_stack = jnp.stack(key_list)
    value_stack = jnp.stack(value_list)
    clip_stack = jnp.stack(clip_list)

    blocks = key_stack.shape[0]
    window_row = lax.dynamic_index_in_dim(neighbours, position, 0, keepdims=False)
    sources = position - jnp.asarray(offsets, dtype=jnp.int32)
    present = jnp.any(
        (window_row[None, :] == sources[:, None]) & (window_row[None, :] >= 0), axis=1
    )
    key_clips = clip_stack.reshape(blocks * tile_rows)
    allowed = jnp.repeat(present, tile_rows)[None, :] & (clip_ids[:, None] == key_clips[None, :])
    key_rows = key_stack.reshape(blocks * tile_rows, feature_width)
    value_rows = value_stack.reshape(blocks * tile_rows, feature_width)
    head_outputs = []
    for head_index in range(feature_width // HD):
        first_col = head_index * HD
        head_outputs.append(
            attend_head(
                queries[:, first_col : first_col + HD],
                key_rows[:, first_col : first_col + HD],
                value_rows[:, first_col : first_col + HD],
                allowed,
            )
        )
    attended = jnp.concatenate(head_outputs, axis=1)

    features = exchange_heads(attended)
    regrouped = features.reshape(tile_rows, seq_count, rep_count, part_rows)
    regrouped = jnp.swapaxes(regrouped, 1, 2).reshape(tile_rows, features.shape[1])
    projected = jnp.dot(regrouped, both_parts, preferred_element_type=jnp.float32)
    return projected.astype(jnp.bfloat16)


def solution(mesh):
    in_specs = (
        P(("rep", "seq"), "head"),
        P(("rep", "seq"), "head"),
        P(("rep", "seq"), "head"),
        P("seq", "head"),
        P("rep", None),
        P(("rep", "seq")),
    )
    out_specs = P(("rep", "seq"), "head")
    return jax.shard_map(
        on_device, mesh=mesh, in_specs=in_specs, out_specs=out_specs, check_vma=False
    )
```

```python
import math

import jax
import jax.numpy as jnp
from jax import lax
from jax.sharding import PartitionSpec as P

HD = 128
TGH = 4
TGW = 7


def from_behind(value, axis, by):
    peers = lax.axis_size(axis)
    pairs = [(i, i + by) for i in range(peers) if 0 <= i + by < peers]
    return lax.ppermute(value, axis, pairs)


def attend_head(query_head, key_head, value_head, allowed):
    scores = lax.dot_general(
        query_head, key_head, (((1,), (1,)), ((), ())), preferred_element_type=jnp.float32
    ) * (1.0 / math.sqrt(query_head.shape[1]))
    masked = jnp.where(allowed, scores, -1e30)
    highest = jnp.max(masked, axis=1, keepdims=True)
    raised = jnp.where(allowed, jnp.exp(masked - highest), 0.0)
    summed = jnp.sum(raised, axis=1, keepdims=True)
    weights = (raised / summed).astype(jnp.bfloat16)
    return jnp.dot(weights, value_head, preferred_element_type=jnp.float32).astype(jnp.bfloat16)


def exchange_heads(attended):
    head_count = lax.axis_size("head")
    head_position = lax.axis_index("head")
    received = [attended]
    for shift in range(1, head_count):
        pairs = [(j, (j + shift) % head_count) for j in range(head_count)]
        received.append(lax.ppermute(attended, "head", pairs))
    ordered = []
    for group in range(head_count):
        block = received[0]
        for shift in range(1, head_count):
            block = jnp.where((head_position - shift) % head_count == group, received[shift], block)
        ordered.append(block)
    return jnp.concatenate(ordered, axis=1)


def on_device(queries, keys, values, out_weight, neighbours, clip_ids):
    tile_rows = queries.shape[0]
    feature_width = queries.shape[1]
    seq_count = lax.axis_size("seq")
    position = lax.axis_index("seq")
    rep_position = lax.axis_index("rep")
    layer_tiles = TGH * TGW
    every_offset = set()
    for layer_step in (-1, 0, 1):
        for row_step in (-1, 0, 1):
            for col_step in (-1, 0, 1):
                every_offset.add(layer_step * layer_tiles + row_step * TGW + col_step)
    distances = [offset for offset in sorted(every_offset) if 0 < offset < seq_count]

    rep_count = lax.axis_size("rep")
    part_rows = out_weight.shape[0] // rep_count
    own_part = jnp.take(
        out_weight.reshape(rep_count, part_rows, out_weight.shape[1]), rep_position, axis=0
    )
    both_parts = lax.all_gather(own_part, ("rep", "seq"), axis=0, tiled=True)

    key_list = [keys]
    value_list = [values]
    clip_list = [clip_ids]
    offsets = [0]
    for distance in distances:
        below_keys, below_values, below_clips = from_behind(
            (keys, values, clip_ids), "seq", distance
        )
        above_keys, above_values, above_clips = from_behind(
            (keys, values, clip_ids), "seq", -distance
        )
        key_list += [below_keys, above_keys]
        value_list += [below_values, above_values]
        clip_list += [below_clips, above_clips]
        offsets += [distance, -distance]
    key_stack = jnp.stack(key_list)
    value_stack = jnp.stack(value_list)
    clip_stack = jnp.stack(clip_list)

    blocks = key_stack.shape[0]
    window_row = lax.dynamic_index_in_dim(neighbours, position, 0, keepdims=False)
    sources = position - jnp.asarray(offsets, dtype=jnp.int32)
    present = jnp.any(
        (window_row[None, :] == sources[:, None]) & (window_row[None, :] >= 0), axis=1
    )
    key_clips = clip_stack.reshape(blocks * tile_rows)
    allowed = jnp.repeat(present, tile_rows)[None, :] & (clip_ids[:, None] == key_clips[None, :])
    key_rows = key_stack.reshape(blocks * tile_rows, feature_width)
    value_rows = value_stack.reshape(blocks * tile_rows, feature_width)
    head_outputs = []
    for head_index in range(feature_width // HD):
        first_col = head_index * HD
        head_outputs.append(
            attend_head(
                queries[:, first_col : first_col + HD],
                key_rows[:, first_col : first_col + HD],
                value_rows[:, first_col : first_col + HD],
                allowed,
            )
        )
    attended = jnp.concatenate(head_outputs, axis=1)

    features = exchange_heads(attended)
    regrouped = features.reshape(tile_rows, seq_count, rep_count, part_rows)
    regrouped = jnp.swapaxes(regrouped, 1, 2).reshape(tile_rows, features.shape[1])
    projected = jnp.dot(regrouped, both_parts, preferred_element_type=jnp.float32)
    return projected.astype(jnp.bfloat16)


def solution(mesh):
    in_specs = (
        P(("rep", "seq"), "head"),
        P(("rep", "seq"), "head"),
        P(("rep", "seq"), "head"),
        P("seq", "head"),
        P("rep", None),
        P(("rep", "seq")),
    )
    out_specs = P(("rep", "seq"), "head")
    return jax.shard_map(
        on_device, mesh=mesh, in_specs=in_specs, out_specs=out_specs, check_vma=False
    )
```
